128 devices in a mesh: occ: 8 (over z_hi, x), vir: 16 (over z_lo, y, core).
Axes of the slice: x: 4, y: 4, z: 4 (z_hi: 2, z_lo: 2; z = z_hi * 2 + z_lo), core: 2. Of those that a mesh axis runs over, the one named last changes fastest.
Arguments:
- amplitudes: float32 [512, 10240], P('vir', 'occ'), may hold values from -12 to 12
- integrals: float32 [10240, 10240], P('occ', 'vir'), may hold values from -0.0625 to 0.0625
Outputs:
- ladder: float32 [512, 10240], P('occ', 'vir')
The draws below stay inside these ranges and needn't reach their ends.
All inputs are finite; a program needn't handle non-finite values.
Results may differ from the reference program's by a relative error of at most 0.00007.
Values sent between devices are 32-bit elements; how exact they have to be, the bound alone decides.
No kernel may reach another device: no remote copies, remote signals or barrier semaphores. Data moves between devices by JAX's collectives and lax.ppermute only.
A program may use at most 64 MiB of HBM per device.

```python
import jax
import jax.numpy as jnp
from jax import lax

CD = 10240
AB = 10240
ROWS = 512


def raised(entries, stream_key, source, target, parts, factor):
    owner, partner = [(jnp.arange(entries.shape[axis_at]) // (entries.shape[axis_at] // parts)).reshape([-1 if axis == axis_at else 1 for axis in range(entries.ndim)]) for axis_at in (source, target)]
    chosen = jax.random.permutation(stream_key, parts)[partner]
    strong = (owner == chosen) | (owner == (partner + parts // 2) % parts)
    return jnp.where(strong, factor * entries, entries)


def block_scale(own_key, shape, shards, least, high):
    gain = 1.0
    for position, blocks in shards:
        draws = jax.random.uniform(jax.random.fold_in(jax.random.fold_in(own_key, 6), position), (blocks,), jnp.float32, least / len(shards), high / len(shards))
        gain = gain * jnp.repeat(jnp.exp(draws), shape[position] // blocks).reshape((-1,) + (1,) * (len(shape) - 1 - position))
    return gain


def noise(rng, extent, spread, limit, pieces=(), dtype=jnp.bfloat16):
    array = spread * jax.random.normal(rng, extent, jnp.float32)
    if pieces:
        array = array * block_scale(rng, extent, pieces, -0.22, 0.18)
    return jnp.clip(array, -limit, limit).astype(dtype)


def noise_with(stream_key, dims, deviation, most, cuts, heavy, kind=jnp.bfloat16):
    drawn = deviation * jax.random.normal(stream_key, dims, jnp.float32)
    if cuts:
        drawn = drawn * block_scale(stream_key, dims, cuts, -0.22, 0.18)
    return jnp.clip(raised(drawn, jax.random.fold_in(stream_key, 3), *heavy), -most, most).astype(kind)


def setup_inputs(seed: int = 0) -> dict:
    keys = jax.random.split(jax.random.key(seed), 3)
    amplitudes = noise_with(keys[0], (ROWS, CD), 2.0, 12.0, ((0, 16), (1, 8)), (1, 0, 16, 2.0), jnp.float32)
    integrals = noise(keys[1], (CD, AB), CD ** -0.5, 0.0625, ((0, 8), (1, 16)), jnp.float32)
    return {"amplitudes": amplitudes, "integrals": integrals}


def reference(amplitudes, integrals):
    contracted = jnp.dot(amplitudes, integrals, preferred_element_type=jnp.float32, precision=lax.Precision.HIGHEST)
    return 0.5 * contracted
```

```python
import jax
import jax.numpy as jnp
from jax import lax
from jax.sharding import PartitionSpec as P

HIGHEST = lax.Precision.HIGHEST


def _pairs(n, dest):
    return [(k, dest(k)) for k in range(n)]


def make_body(n_occ, n_vir):
    ny = n_vir // 4
    nx = n_occ // 2

    def vir_of(zl, y, c):
        return zl * (2 * ny) + y * 2 + c

    def vir_split(j):
        return j // (2 * ny), (j // 2) % ny, j % 2

    def y_shift(s):
        def dest(j):
            zl, y, c = vir_split(j)
            return vir_of(zl, (y + s) % ny, c)

        return _pairs(n_vir, dest)

    def x_shift(s):
        return _pairs(n_occ, lambda i: (i // nx) * nx + (i % nx + s) % nx)

    z_swap = _pairs(n_vir, lambda j: j ^ (2 * ny))
    core_swap = _pairs(n_vir, lambda j: j ^ 1)
    zhi_swap = _pairs(n_occ, lambda i: (i + nx) % n_occ)

    def body(amplitudes, integrals):
        rows, cd = amplitudes.shape
        me = lax.axis_index("vir")
        zl, y, c = me // (2 * ny), (me // 2) % ny, me % 2

        b_z = lax.ppermute(amplitudes, "vir", z_swap)
        pair = jnp.concatenate([amplitudes, b_z], axis=0)
        from_m = lax.ppermute(pair, "vir", y_shift(1))
        from_p = lax.ppermute(pair, "vir", y_shift(-1))
        far_m = lax.ppermute(from_m[:rows], "vir", y_shift(1))
        far_p = lax.ppermute(from_p[rows:], "vir", y_shift(-1))
        local = jnp.concatenate([amplitudes, b_z, from_m, from_p, far_m, far_p], axis=0)
        other = lax.ppermute(local, "vir", core_swap)
        offsets = [(0, 0), (0, 1), (-1, 0), (-1, 1), (1, 0), (1, 1), (2, 0), (2, 1)]
        full = jnp.zeros((n_vir, rows, cd), amplitudes.dtype)
        for k, (dy, dz) in enumerate(offsets):
            base = (zl ^ dz) * (2 * ny) + ((y + dy) % ny) * 2
            full = lax.dynamic_update_index_in_dim(full, local[k * rows:(k + 1) * rows], base + c, 0)
            full = lax.dynamic_update_index_in_dim(full, other[k * rows:(k + 1) * rows], base + (1 - c), 0)
        full = full.reshape(n_vir * rows, cd)

        partial = 0.5 * jnp.dot(
            full, integrals, preferred_element_type=jnp.float32, precision=HIGHEST
        )

        mo = lax.axis_index("occ")
        x, zh = mo % nx, mo // nx
        blocks = partial.reshape(n_occ, -1, partial.shape[1])

        def a_blk(t):
            return lax.dynamic_index_in_dim(blocks, t % nx, 0, keepdims=False)

        def b_blk(t):
            return lax.dynamic_index_in_dim(blocks, nx + t % nx, 0, keepdims=False)

        sa = a_blk(x - 1 + nx)
        sb = b_blk(x + 1)
        for s in range(1, nx):
            sa = lax.ppermute(sa, "occ", x_shift(1)) + a_blk(x - s - 1 + 2 * nx)
            sb = lax.ppermute(sb, "occ", x_shift(-1)) + b_blk(x + s + 1)
        keep = jnp.where(zh == 0, sa, sb)
        send = jnp.where(zh == 0, sb, sa)
        return keep + lax.ppermute(send, "occ", zhi_swap)

    return body


def solution(mesh):
    placed = (P("vir", "occ"), P("occ", "vir"))
    return jax.shard_map(
        make_body(mesh.shape["occ"], mesh.shape["vir"]),
        mesh=mesh,
        in_specs=placed,
        out_specs=P("occ", "vir"),
        check_vma=False,
    )
```

```python
import jax
import jax.numpy as jnp
from jax import lax
from jax.sharding import PartitionSpec as P

HIGHEST = lax.Precision.HIGHEST


def _pairs(n, dest):
    return [(k, dest(k)) for k in range(n)]


def make_body(n_occ, n_vir):
    ny = n_vir // 4
    nx = n_occ // 2

    def y_shift(s):
        def dest(j):
            zl, y, c = j // (2 * ny), (j // 2) % ny, j % 2
            return zl * (2 * ny) + ((y + s) % ny) * 2 + c

        return _pairs(n_vir, dest)

    def x_shift(s):
        return _pairs(n_occ, lambda i: (i // nx) * nx + (i % nx + s) % nx)

    z_swap = _pairs(n_vir, lambda j: j ^ (2 * ny))
    core_swap = _pairs(n_vir, lambda j: j ^ 1)
    zhi_swap = _pairs(n_occ, lambda i: (i + nx) % n_occ)
    slot_of = [0, 1, 3, 4, 5, 7, 2, 6]

    def matmul(a, b):
        return jnp.dot(a, b, preferred_element_type=jnp.float32, precision=HIGHEST)

    def body(amplitudes, integrals):
        rows, cd = amplitudes.shape
        me = lax.axis_index("vir")
        zl, y, c = me // (2 * ny), (me // 2) % ny, me % 2

        own = amplitudes
        z1 = lax.ppermute(own, "vir", z_swap)
        ym1 = lax.ppermute(own, "vir", y_shift(1))
        yp1 = lax.ppermute(own, "vir", y_shift(-1))
        z2 = lax.ppermute(yp1, "vir", z_swap)
        yp2 = lax.ppermute(yp1, "vir", y_shift(-1))
        ym1z = lax.ppermute(z1, "vir", y_shift(1))
        z3 = lax.ppermute(yp2, "vir", z_swap)
        local = jnp.concatenate([own, z1, ym1, yp1, z2, yp2, ym1z, z3], axis=0)
        other = lax.ppermute(local, "vir", core_swap)
        res_l = (0.5 * matmul(local, integrals)).reshape(8, rows, -1)
        res_o = (0.5 * matmul(other, integrals)).reshape(8, rows, -1)
        table = jnp.array(slot_of, jnp.int32)

        def out_block(r):
            dy = (r % nx - y) % ny
            dz = (r // nx) ^ zl
            k = table[dy * 2 + dz]
            lk = lax.dynamic_index_in_dim(res_l, k, 0, keepdims=False)
            ok = lax.dynamic_index_in_dim(res_o, k, 0, keepdims=False)
            first = jnp.where(c == 0, lk, ok)
            second = jnp.where(c == 0, ok, lk)
            return jnp.concatenate([first, second], axis=0)

        mo = lax.axis_index("occ")
        x, zh = mo % nx, mo // nx
        sa = out_block((x - 1) % nx)
        sb = out_block(nx + (x + 1) % nx)
        for s in range(1, nx):
            sa = lax.ppermute(sa, "occ", x_shift(1)) + out_block((x - s - 1) % nx)
            sb = lax.ppermute(sb, "occ", x_shift(-1)) + out_block(nx + (x + s + 1) % nx)
        keep = jnp.where(zh == 0, sa, sb)
        send = jnp.where(zh == 0, sb, sa)
        return keep + lax.ppermute(send, "occ", zhi_swap)

    return body


def solution(mesh):
    placed = (P("vir", "occ"), P("occ", "vir"))
    return jax.shard_map(
        make_body(mesh.shape["occ"], mesh.shape["vir"]),
        mesh=mesh,
        in_specs=placed,
        out_specs=P("occ", "vir"),
        check_vma=False,
    )
```

```python
import jax
import jax.numpy as jnp
from jax import lax
from jax.experimental import pallas as pl
from jax.experimental.pallas import tpu as pltpu
from jax.sharding import PartitionSpec as P

HIGHEST = lax.Precision.HIGHEST


def _pairs(n, dest):
    return [(k, dest(k)) for k in range(n)]


def _matmul_kernel(a_ref, b_ref, o_ref):
    @pl.when(pl.program_id(0) == 0)
    def _():
        o_ref[...] = jnp.zeros_like(o_ref)

    o_ref[...] += jnp.dot(
        a_ref[...], b_ref[...], preferred_element_type=jnp.float32, precision=HIGHEST
    )


def _stream_matmul(a, b, tk=256):
    m, k = a.shape
    n = b.shape[1]
    return pl.pallas_call(
        _matmul_kernel,
        out_shape=jax.ShapeDtypeStruct((m, n), jnp.float32),
        grid=(k // tk,),
        in_specs=[
            pl.BlockSpec((m, tk), lambda i: (0, i)),
            pl.BlockSpec((tk, n), lambda i: (i, 0)),
        ],
        out_specs=pl.BlockSpec((m, n), lambda i: (0, 0)),
        cost_estimate=pl.CostEstimate(
            flops=2 * m * n * k, transcendentals=0, bytes_accessed=4 * (m * k + k * n + m * n)
        ),
    )(a, b)


def make_body(n_occ, n_vir):
    ny = n_vir // 4
    nx = n_occ // 2

    def y_shift(s):
        def dest(j):
            zl, y, c = j // (2 * ny), (j // 2) % ny, j % 2
            return zl * (2 * ny) + ((y + s) % ny) * 2 + c

        return _pairs(n_vir, dest)

    def x_shift(s):
        return _pairs(n_occ, lambda i: (i // nx) * nx + (i % nx + s) % nx)

    z_swap = _pairs(n_vir, lambda j: j ^ (2 * ny))
    core_swap = _pairs(n_vir, lambda j: j ^ 1)
    zhi_swap = _pairs(n_occ, lambda i: (i + nx) % n_occ)
    slot_of = [0, 1, 3, 4, 5, 7, 2, 6]

    def matmul(a, b):
        return _stream_matmul(a, b)

    def body(amplitudes, integrals):
        rows, cd = amplitudes.shape
        me = lax.axis_index("vir")
        zl, y, c = me // (2 * ny), (me // 2) % ny, me % 2

        own = amplitudes
        z1 = lax.ppermute(own, "vir", z_swap)
        ym1 = lax.ppermute(own, "vir", y_shift(1))
        yp1 = lax.ppermute(own, "vir", y_shift(-1))
        z2 = lax.ppermute(yp1, "vir", z_swap)
        yp2 = lax.ppermute(yp1, "vir", y_shift(-1))
        ym1z = lax.ppermute(z1, "vir", y_shift(1))
        z3 = lax.ppermute(yp2, "vir", z_swap)
        local = jnp.concatenate([own, z1, ym1, yp1, z2, yp2, ym1z, z3], axis=0)
        other = lax.ppermute(local, "vir", core_swap)
        res_l = (0.5 * matmul(local, integrals)).reshape(8, rows, -1)
        res_o = (0.5 * matmul(other, integrals)).reshape(8, rows, -1)
        table = jnp.array(slot_of, jnp.int32)

        def out_block(r):
            dy = (r % nx - y) % ny
            dz = (r // nx) ^ zl
            k = table[dy * 2 + dz]
            lk = lax.dynamic_index_in_dim(res_l, k, 0, keepdims=False)
            ok = lax.dynamic_index_in_dim(res_o, k, 0, keepdims=False)
            first = jnp.where(c == 0, lk, ok)
            second = jnp.where(c == 0, ok, lk)
            return jnp.concatenate([first, second], axis=0)

        mo = lax.axis_index("occ")
        x, zh = mo % nx, mo // nx
        sa = out_block((x - 1) % nx)
        sb = out_block(nx + (x + 1) % nx)
        for s in range(1, nx):
            sa = lax.ppermute(sa, "occ", x_shift(1)) + out_block((x - s - 1) % nx)
            sb = lax.ppermute(sb, "occ", x_shift(-1)) + out_block(nx + (x + s + 1) % nx)
        keep = jnp.where(zh == 0, sa, sb)
        send = jnp.where(zh == 0, sb, sa)
        return keep + lax.ppermute(send, "occ", zhi_swap)

    return body


def solution(mesh):
    placed = (P("vir", "occ"), P("occ", "vir"))
    return jax.shard_map(
        make_body(mesh.shape["occ"], mesh.shape["vir"]),
        mesh=mesh,
        in_specs=placed,
        out_specs=P("occ", "vir"),
        check_vma=False,
    )
```

```python
import jax
import jax.numpy as jnp
from jax import lax
from jax.sharding import PartitionSpec as P

HIGH = lax.Precision.HIGH


def _pairs(n, dest):
    return [(k, dest(k)) for k in range(n)]


def make_body(n_occ, n_vir):
    ny = n_vir // 4
    nx = n_occ // 2

    def y_shift(s):
        def dest(j):
            zl, y, c = j // (2 * ny), (j // 2) % ny, j % 2
            return zl * (2 * ny) + ((y + s) % ny) * 2 + c

        return _pairs(n_vir, dest)

    def x_shift(s):
        return _pairs(n_occ, lambda i: (i // nx) * nx + (i % nx + s) % nx)

    z_swap = _pairs(n_vir, lambda j: j ^ (2 * ny))
    core_swap = _pairs(n_vir, lambda j: j ^ 1)
    zhi_swap = _pairs(n_occ, lambda i: (i + nx) % n_occ)
    slot_of = [0, 1, 3, 4, 5, 7, 2, 6]

    def matmul(a, b):
        return jnp.dot(a, b, preferred_element_type=jnp.float32, precision=HIGH)

    def body(amplitudes, integrals):
        rows, cd = amplitudes.shape
        me = lax.axis_index("vir")
        zl, y, c = me // (2 * ny), (me // 2) % ny, me % 2

        half = 0.5 * integrals
        res_own = matmul(amplitudes, half)
        own, res_own = lax.optimization_barrier((amplitudes, res_own))
        z1 = lax.ppermute(own, "vir", z_swap)
        ym1 = lax.ppermute(own, "vir", y_shift(1))
        yp1 = lax.ppermute(own, "vir", y_shift(-1))
        z2 = lax.ppermute(yp1, "vir", z_swap)
        yp2 = lax.ppermute(yp1, "vir", y_shift(-1))
        ym1z = lax.ppermute(z1, "vir", y_shift(1))
        z3 = lax.ppermute(yp2, "vir", z_swap)
        local = jnp.concatenate([own, z1, ym1, yp1, z2, yp2, ym1z, z3], axis=0)
        other = lax.ppermute(local, "vir", core_swap)
        res_l = jnp.concatenate([res_own, matmul(local[rows:], half)], axis=0).reshape(8, rows, -1)
        res_o = matmul(other, half).reshape(8, rows, -1)
        table = jnp.array(slot_of, jnp.int32)

        def out_block(r):
            dy = (r % nx - y) % ny
            dz = (r // nx) ^ zl
            k = table[dy * 2 + dz]
            lk = lax.dynamic_index_in_dim(res_l, k, 0, keepdims=False)
            ok = lax.dynamic_index_in_dim(res_o, k, 0, keepdims=False)
            first = jnp.where(c == 0, lk, ok)
            second = jnp.where(c == 0, ok, lk)
            return jnp.concatenate([first, second], axis=0)

        mo = lax.axis_index("occ")
        x, zh = mo % nx, mo // nx
        sa = out_block((x - 1) % nx)
        sb = out_block(nx + (x + 1) % nx)
        for s in range(1, nx):
            sa = lax.ppermute(sa, "occ", x_shift(1)) + out_block((x - s - 1) % nx)
            sb = lax.ppermute(sb, "occ", x_shift(-1)) + out_block(nx + (x + s + 1) % nx)
        keep = jnp.where(zh == 0, sa, sb)
        send = jnp.where(zh == 0, sb, sa)
        return keep + lax.ppermute(send, "occ", zhi_swap)

    return body


def solution(mesh):
    placed = (P("vir", "occ"), P("occ", "vir"))
    return jax.shard_map(
        make_body(mesh.shape["occ"], mesh.shape["vir"]),
        mesh=mesh,
        in_specs=placed,
        out_specs=P("occ", "vir"),
        check_vma=False,
    )
```

```python
import jax
import jax.numpy as jnp
from jax import lax
from jax.sharding import PartitionSpec as P

HIGH = lax.Precision.HIGH


def _pairs(n, dest):
    return [(k, dest(k)) for k in range(n)]


def make_body(n_occ, n_vir):
    ny = n_vir // 4
    nx = n_occ // 2

    def y_shift(s):
        def dest(j):
            zl, y, c = j // (2 * ny), (j // 2) % ny, j % 2
            return zl * (2 * ny) + ((y + s) % ny) * 2 + c

        return _pairs(n_vir, dest)

    def x_shift(s):
        return _pairs(n_occ, lambda i: (i // nx) * nx + (i % nx + s) % nx)

    z_swap = _pairs(n_vir, lambda j: j ^ (2 * ny))
    core_swap = _pairs(n_vir, lambda j: j ^ 1)
    zhi_swap = _pairs(n_occ, lambda i: (i + nx) % n_occ)
    slot_of = [0, 1, 3, 4, 5, 7, 2, 6]

    def matmul(a, b):
        return jnp.dot(a, b, preferred_element_type=jnp.float32, precision=HIGH)

    def body(amplitudes, integrals):
        rows, cd = amplitudes.shape
        me = lax.axis_index("vir")
        zl, y, c = me // (2 * ny), (me // 2) % ny, me % 2

        half = 0.5 * integrals
        res_own = matmul(amplitudes, half)
        own, res_own = lax.optimization_barrier((amplitudes, res_own))
        z1 = lax.ppermute(own, "vir", z_swap)
        ym1 = lax.ppermute(own, "vir", y_shift(1))
        yp1 = lax.ppermute(own, "vir", y_shift(-1))
        z2 = lax.ppermute(yp1, "vir", z_swap)
        yp2 = lax.ppermute(yp1, "vir", y_shift(-1))
        ym1z = lax.ppermute(z1, "vir", y_shift(1))
        z3 = lax.ppermute(yp2, "vir", z_swap)
        local = jnp.concatenate([own, z1, ym1, yp1, z2, yp2, ym1z, z3], axis=0)
        res_l = jnp.concatenate([res_own, matmul(local[rows:], half)], axis=0)
        local, res_l = lax.optimization_barrier((local, res_l))
        res_l = res_l.reshape(8, rows, -1)
        other = lax.ppermute(local, "vir", core_swap)
        res_o = matmul(other, half).reshape(8, rows, -1)
        table = jnp.array(slot_of, jnp.int32)

        def out_block(r):
            dy = (r % nx - y) % ny
            dz = (r // nx) ^ zl
            k = table[dy * 2 + dz]
            lk = lax.dynamic_index_in_dim(res_l, k, 0, keepdims=False)
            ok = lax.dynamic_index_in_dim(res_o, k, 0, keepdims=False)
            first = jnp.where(c == 0, lk, ok)
            second = jnp.where(c == 0, ok, lk)
            return jnp.concatenate([first, second], axis=0)

        mo = lax.axis_index("occ")
        x, zh = mo % nx, mo // nx
        sa = out_block((x - 1) % nx)
        sb = out_block(nx + (x + 1) % nx)
        for s in range(1, nx):
            sa = lax.ppermute(sa, "occ", x_shift(1)) + out_block((x - s - 1) % nx)
            sb = lax.ppermute(sb, "occ", x_shift(-1)) + out_block(nx + (x + s + 1) % nx)
        keep = jnp.where(zh == 0, sa, sb)
        send = jnp.where(zh == 0, sb, sa)
        return keep + lax.ppermute(send, "occ", zhi_swap)

    return body


def solution(mesh):
    placed = (P("vir", "occ"), P("occ", "vir"))
    return jax.shard_map(
        make_body(mesh.shape["occ"], mesh.shape["vir"]),
        mesh=mesh,
        in_specs=placed,
        out_specs=P("occ", "vir"),
        check_vma=False,
    )
```

```python
import jax
import jax.numpy as jnp
from jax import lax
from jax.sharding import PartitionSpec as P

HIGH = lax.Precision.HIGH


def _pairs(n, dest):
    return [(k, dest(k)) for k in range(n)]


def make_body(n_occ, n_vir):
    ny = n_vir // 4
    nx = n_occ // 2

    def y_shift(s):
        def dest(j):
            zl, y, c = j // (2 * ny), (j // 2) % ny, j % 2
            return zl * (2 * ny) + ((y + s) % ny) * 2 + c

        return _pairs(n_vir, dest)

    def x_shift(s):
        return _pairs(n_occ, lambda i: (i // nx) * nx + (i % nx + s) % nx)

    z_swap = _pairs(n_vir, lambda j: j ^ (2 * ny))
    core_swap = _pairs(n_vir, lambda j: j ^ 1)
    zhi_swap = _pairs(n_occ, lambda i: (i + nx) % n_occ)
    slot_of = [0, 1, 3, 4, 5, 7, 2, 6]

    def matmul(a, b):
        return jnp.dot(a, b, preferred_element_type=jnp.float32, precision=HIGH)

    def body(amplitudes, integrals):
        rows, cd = amplitudes.shape
        me = lax.axis_index("vir")
        zl, y, c = me // (2 * ny), (me // 2) % ny, me % 2

        half = 0.5 * integrals
        res_own = matmul(amplitudes, half)
        own, res_own = lax.optimization_barrier((amplitudes, res_own))
        z1 = lax.ppermute(own, "vir", z_swap)
        ym1 = lax.ppermute(own, "vir", y_shift(1))
        yp1 = lax.ppermute(own, "vir", y_shift(-1))
        first = jnp.concatenate([own, z1, ym1, yp1], axis=0)
        other_first = lax.ppermute(first, "vir", core_swap)
        z2 = lax.ppermute(yp1, "vir", z_swap)
        yp2 = lax.ppermute(yp1, "vir", y_shift(-1))
        ym1z = lax.ppermute(z1, "vir", y_shift(1))
        second = jnp.concatenate([z2, yp2, ym1z], axis=0)
        other_second = lax.ppermute(second, "vir", core_swap)
        z3 = lax.ppermute(yp2, "vir", z_swap)
        local = jnp.concatenate([first, second, z3], axis=0)
        res_l = jnp.concatenate([res_own, matmul(local[rows:], half)], axis=0)
        z3, res_l = lax.optimization_barrier((z3, res_l))
        res_l = res_l.reshape(8, rows, -1)
        other_last = lax.ppermute(z3, "vir", core_swap)
        other = jnp.concatenate([other_first, other_second, other_last], axis=0)
        res_o = matmul(other, half).reshape(8, rows, -1)
        table = jnp.array(slot_of, jnp.int32)

        def out_block(r):
            dy = (r % nx - y) % ny
            dz = (r // nx) ^ zl
            k = table[dy * 2 + dz]
            lk = lax.dynamic_index_in_dim(res_l, k, 0, keepdims=False)
            ok = lax.dynamic_index_in_dim(res_o, k, 0, keepdims=False)
            first = jnp.where(c == 0, lk, ok)
            second = jnp.where(c == 0, ok, lk)
            return jnp.concatenate([first, second], axis=0)

        mo = lax.axis_index("occ")
        x, zh = mo % nx, mo // nx
        sa = out_block((x - 1) % nx)
        sb = out_block(nx + (x + 1) % nx)
        for s in range(1, nx):
            sa = lax.ppermute(sa, "occ", x_shift(1)) + out_block((x - s - 1) % nx)
            sb = lax.ppermute(sb, "occ", x_shift(-1)) + out_block(nx + (x + s + 1) % nx)
        keep = jnp.where(zh == 0, sa, sb)
        send = jnp.where(zh == 0, sb, sa)
        return keep + lax.ppermute(send, "occ", zhi_swap)

    return body


def solution(mesh):
    placed = (P("vir", "occ"), P("occ", "vir"))
    return jax.shard_map(
        make_body(mesh.shape["occ"], mesh.shape["vir"]),
        mesh=mesh,
        in_specs=placed,
        out_specs=P("occ", "vir"),
        check_vma=False,
    )
```

```python
import jax
import jax.numpy as jnp
from jax import lax
from jax.sharding import PartitionSpec as P

HIGH = lax.Precision.HIGH


def _pairs(n, dest):
    return [(k, dest(k)) for k in range(n)]


def make_body(n_occ, n_vir):
    ny = n_vir // 4
    nx = n_occ // 2

    def y_shift(s):
        def dest(j):
            zl, y, c = j // (2 * ny), (j // 2) % ny, j % 2
            return zl * (2 * ny) + ((y + s) % ny) * 2 + c

        return _pairs(n_vir, dest)

    def x_shift(s):
        return _pairs(n_occ, lambda i: (i // nx) * nx + (i % nx + s) % nx)

    z_swap = _pairs(n_vir, lambda j: j ^ (2 * ny))
    core_swap = _pairs(n_vir, lambda j: j ^ 1)
    zhi_swap = _pairs(n_occ, lambda i: (i + nx) % n_occ)
    slot_of = [0, 1, 4, 5, 6, 7, 2, 3]

    def matmul(a, b):
        return jnp.dot(a, b, preferred_element_type=jnp.float32, precision=HIGH)

    def body(amplitudes, integrals):
        rows, cd = amplitudes.shape
        me = lax.axis_index("vir")
        zl, y, c = me // (2 * ny), (me // 2) % ny, me % 2

        half = 0.5 * integrals
        res_own = matmul(amplitudes, half)
        own, res_own = lax.optimization_barrier((amplitudes, res_own))
        z1 = lax.ppermute(own, "vir", z_swap)
        pair = jnp.concatenate([own, z1], axis=0)
        from_m = lax.ppermute(pair, "vir", y_shift(1))
        from_p = lax.ppermute(pair, "vir", y_shift(-1))
        far_m = lax.ppermute(from_m[:rows], "vir", y_shift(1))
        far_p = lax.ppermute(from_p[rows:], "vir", y_shift(-1))
        local = jnp.concatenate([own, z1, from_m, from_p, far_m, far_p], axis=0)
        res_l = jnp.concatenate([res_own, matmul(local[rows:], half)], axis=0)
        local, res_l = lax.optimization_barrier((local, res_l))
        res_l = res_l.reshape(8, rows, -1)
        other = lax.ppermute(local, "vir", core_swap)
        res_o = matmul(other, half).reshape(8, rows, -1)
        table = jnp.array(slot_of, jnp.int32)

        def out_block(r):
            dy = (r % nx - y) % ny
            dz = (r // nx) ^ zl
            k = table[dy * 2 + dz]
            lk = lax.dynamic_index_in_dim(res_l, k, 0, keepdims=False)
            ok = lax.dynamic_index_in_dim(res_o, k, 0, keepdims=False)
            first = jnp.where(c == 0, lk, ok)
            second = jnp.where(c == 0, ok, lk)
            return jnp.concatenate([first, second], axis=0)

        mo = lax.axis_index("occ")
        x, zh = mo % nx, mo // nx
        sa = out_block((x - 1) % nx)
        sb = out_block(nx + (x + 1) % nx)
        for s in range(1, nx):
            sa = lax.ppermute(sa, "occ", x_shift(1)) + out_block((x - s - 1) % nx)
            sb = lax.ppermute(sb, "occ", x_shift(-1)) + out_block(nx + (x + s + 1) % nx)
        keep = jnp.where(zh == 0, sa, sb)
        send = jnp.where(zh == 0, sb, sa)
        return keep + lax.ppermute(send, "occ", zhi_swap)

    return body


def solution(mesh):
    placed = (P("vir", "occ"), P("occ", "vir"))
    return jax.shard_map(
        make_body(mesh.shape["occ"], mesh.shape["vir"]),
        mesh=mesh,
        in_specs=placed,
        out_specs=P("occ", "vir"),
        check_vma=False,
    )
```

```python
import jax
import jax.numpy as jnp
from jax import lax
from jax.sharding import PartitionSpec as P

HIGH = lax.Precision.HIGH


def _pairs(n, dest):
    return [(k, dest(k)) for k in range(n)]


def make_body(n_occ, n_vir):
    ny = n_vir // 4
    nx = n_occ // 2

    def y_shift(s):
        def dest(j):
            zl, y, c = j // (2 * ny), (j // 2) % ny, j % 2
            return zl * (2 * ny) + ((y + s) % ny) * 2 + c

        return _pairs(n_vir, dest)

    def x_shift(s):
        return _pairs(n_occ, lambda i: (i // nx) * nx + (i % nx + s) % nx)

    z_swap = _pairs(n_vir, lambda j: j ^ (2 * ny))
    core_swap = _pairs(n_vir, lambda j: j ^ 1)
    zhi_swap = _pairs(n_occ, lambda i: (i + nx) % n_occ)
    slot_of = [0, 1, 3, 4, 5, 7, 2, 6]

    def matmul(a, b):
        return jnp.dot(a, b, preferred_element_type=jnp.float32, precision=HIGH)

    def body(amplitudes, integrals):
        rows, cd = amplitudes.shape
        me = lax.axis_index("vir")
        zl, y, c = me // (2 * ny), (me // 2) % ny, me % 2

        half = 0.5 * integrals
        res_own = matmul(amplitudes, half)
        own, res_own = lax.optimization_barrier((amplitudes, res_own))
        z1 = lax.ppermute(own, "vir", z_swap)
        ym1 = lax.ppermute(own, "vir", y_shift(1))
        yp1 = lax.ppermute(own, "vir", y_shift(-1))
        z2 = lax.ppermute(yp1, "vir", z_swap)
        yp2 = lax.ppermute(yp1, "vir", y_shift(-1))
        ym1z = lax.ppermute(z1, "vir", y_shift(1))
        z3 = lax.ppermute(yp2, "vir", z_swap)
        local = jnp.concatenate([own, z1, ym1, yp1, z2, yp2, ym1z, z3], axis=0)
        res_l = jnp.concatenate([res_own, matmul(local[rows:], half)], axis=0)
        local, res_l = lax.optimization_barrier((local, res_l))
        res_l = res_l.reshape(8, rows, -1)
        other = lax.ppermute(local, "vir", core_swap)
        table = jnp.array(slot_of, jnp.int32)

        dest = jnp.arange(n_occ, dtype=jnp.int32)
        slots = table[((dest % nx - y) % ny) * 2 + ((dest // nx) ^ zl)]

        def scatter_sum(res):
            parts = jnp.take(res, slots, axis=0)
            return lax.all_to_all(parts, "occ", 0, 0, tiled=False).sum(axis=0)

        sum_l = scatter_sum(res_l)
        other, sum_l = lax.optimization_barrier((other, sum_l))
        res_o = matmul(other, half).reshape(8, rows, -1)
        sum_o = scatter_sum(res_o)
        first = jnp.where(c == 0, sum_l, sum_o)
        second = jnp.where(c == 0, sum_o, sum_l)
        return jnp.concatenate([first, second], axis=0)

    return body


def solution(mesh):
    placed = (P("vir", "occ"), P("occ", "vir"))
    return jax.shard_map(
        make_body(mesh.shape["occ"], mesh.shape["vir"]),
        mesh=mesh,
        in_specs=placed,
        out_specs=P("occ", "vir"),
        check_vma=False,
    )
```

```python
import jax
import jax.numpy as jnp
from jax import lax
from jax.sharding import PartitionSpec as P

HIGH = lax.Precision.HIGH


def _pairs(n, dest):
    return [(k, dest(k)) for k in range(n)]


def make_body(n_occ, n_vir):
    ny = n_vir // 4
    nx = n_occ // 2

    def y_shift(s):
        def dest(j):
            zl, y, c = j // (2 * ny), (j // 2) % ny, j % 2
            return zl * (2 * ny) + ((y + s) % ny) * 2 + c

        return _pairs(n_vir, dest)

    def x_shift(s):
        return _pairs(n_occ, lambda i: (i // nx) * nx + (i % nx + s) % nx)

    z_swap = _pairs(n_vir, lambda j: j ^ (2 * ny))
    core_swap = _pairs(n_vir, lambda j: j ^ 1)
    zhi_swap = _pairs(n_occ, lambda i: (i + nx) % n_occ)
    slot_of = [0, 1, 3, 4, 5, 7, 2, 6]

    def matmul(a, b):
        return jnp.dot(a, b, preferred_element_type=jnp.float32, precision=HIGH)

    def body(amplitudes, integrals):
        rows, cd = amplitudes.shape
        me = lax.axis_index("vir")
        zl, y, c = me // (2 * ny), (me // 2) % ny, me % 2

        half = 0.5 * integrals
        res_own = matmul(amplitudes, half)
        own, res_own = lax.optimization_barrier((amplitudes, res_own))
        z1 = lax.ppermute(own, "vir", z_swap)
        ym1 = lax.ppermute(own, "vir", y_shift(1))
        yp1 = lax.ppermute(own, "vir", y_shift(-1))
        z2 = lax.ppermute(yp1, "vir", z_swap)
        yp2 = lax.ppermute(yp1, "vir", y_shift(-1))
        ym1z = lax.ppermute(z1, "vir", y_shift(1))
        z3 = lax.ppermute(yp2, "vir", z_swap)
        local = jnp.concatenate([own, z1, ym1, yp1, z2, yp2, ym1z, z3], axis=0)
        res_l = jnp.concatenate([res_own, matmul(local[rows:], half)], axis=0)
        local, res_l = lax.optimization_barrier((local, res_l))
        res_l = res_l.reshape(8, rows, -1)
        other = lax.ppermute(local, "vir", core_swap)
        table = jnp.array(slot_of, jnp.int32)
        mo = lax.axis_index("occ")
        x, zh = mo % nx, mo // nx

        def ring(res):
            def half_block(r):
                k = table[((r % nx - y) % ny) * 2 + ((r // nx) ^ zl)]
                return lax.dynamic_index_in_dim(res, k, 0, keepdims=False)

            sa = half_block((x - 1) % nx)
            sb = half_block(nx + (x + 1) % nx)
            for s in range(1, nx):
                sa = lax.ppermute(sa, "occ", x_shift(1)) + half_block((x - s - 1) % nx)
                sb = lax.ppermute(sb, "occ", x_shift(-1)) + half_block(nx + (x + s + 1) % nx)
            keep = jnp.where(zh == 0, sa, sb)
            send = jnp.where(zh == 0, sb, sa)
            return keep + lax.ppermute(send, "occ", zhi_swap)

        sum_l = ring(res_l)
        res_o = matmul(other, half).reshape(8, rows, -1)
        sum_o = ring(res_o)
        first = jnp.where(c == 0, sum_l, sum_o)
        second = jnp.where(c == 0, sum_o, sum_l)
        return jnp.concatenate([first, second], axis=0)

    return body


def solution(mesh):
    placed = (P("vir", "occ"), P("occ", "vir"))
    return jax.shard_map(
        make_body(mesh.shape["occ"], mesh.shape["vir"]),
        mesh=mesh,
        in_specs=placed,
        out_specs=P("occ", "vir"),
        check_vma=False,
    )
```

```python
import jax
import jax.numpy as jnp
from jax import lax
from jax.sharding import PartitionSpec as P

HIGH = lax.Precision.HIGH


def _pairs(n, dest):
    return [(k, dest(k)) for k in range(n)]


def make_body(n_occ, n_vir):
    ny = n_vir // 4
    nx = n_occ // 2

    def y_shift(s):
        def dest(j):
            zl, y, c = j // (2 * ny), (j // 2) % ny, j % 2
            return zl * (2 * ny) + ((y + s) % ny) * 2 + c

        return _pairs(n_vir, dest)

    def x_shift(s):
        return _pairs(n_occ, lambda i: (i // nx) * nx + (i % nx + s) % nx)

    z_swap = _pairs(n_vir, lambda j: j ^ (2 * ny))
    to_odd = [(j, j + 1) for j in range(0, n_vir, 2)]
    to_even = [(j + 1, j) for j in range(0, n_vir, 2)]
    zhi_swap = _pairs(n_occ, lambda i: (i + nx) % n_occ)
    slot_of = [0, 1, 3, 4, 5, 7, 2, 6]

    def matmul(a, b):
        return jnp.dot(a, b, preferred_element_type=jnp.float32, precision=HIGH)

    def body(amplitudes, integrals):
        rows, cd = amplitudes.shape
        me = lax.axis_index("vir")
        zl, y, c = me // (2 * ny), (me // 2) % ny, me % 2

        half = 0.5 * integrals
        res_own = matmul(amplitudes, half)
        own, res_own = lax.optimization_barrier((amplitudes, res_own))
        z1 = lax.ppermute(own, "vir", z_swap)
        ym1 = lax.ppermute(own, "vir", y_shift(1))
        yp1 = lax.ppermute(own, "vir", y_shift(-1))
        z2 = lax.ppermute(yp1, "vir", z_swap)
        yp2 = lax.ppermute(yp1, "vir", y_shift(-1))
        ym1z = lax.ppermute(z1, "vir", y_shift(1))
        z3 = lax.ppermute(yp2, "vir", z_swap)
        local = jnp.concatenate([own, z1, ym1, yp1, z2, yp2, ym1z, z3], axis=0)
        res_l = jnp.concatenate([res_own, matmul(local[rows:], half)], axis=0)
        local, res_l = lax.optimization_barrier((local, res_l))
        res_l = res_l.reshape(8, rows, -1)
        other = lax.ppermute(local, "vir", to_odd) + lax.ppermute(local, "vir", to_even)
        res_o = matmul(other, half).reshape(8, rows, -1)
        table = jnp.array(slot_of, jnp.int32)

        def out_block(r):
            dy = (r % nx - y) % ny
            dz = (r // nx) ^ zl
            k = table[dy * 2 + dz]
            lk = lax.dynamic_index_in_dim(res_l, k, 0, keepdims=False)
            ok = lax.dynamic_index_in_dim(res_o, k, 0, keepdims=False)
            first = jnp.where(c == 0, lk, ok)
            second = jnp.where(c == 0, ok, lk)
            return jnp.concatenate([first, second], axis=0)

        mo = lax.axis_index("occ")
        x, zh = mo % nx, mo // nx
        sa = out_block((x - 1) % nx)
        sb = out_block(nx + (x + 1) % nx)
        for s in range(1, nx):
            sa = lax.ppermute(sa, "occ", x_shift(1)) + out_block((x - s - 1) % nx)
            sb = lax.ppermute(sb, "occ", x_shift(-1)) + out_block(nx + (x + s + 1) % nx)
        keep = jnp.where(zh == 0, sa, sb)
        send = jnp.where(zh == 0, sb, sa)
        return keep + lax.ppermute(send, "occ", zhi_swap)

    return body


def solution(mesh):
    placed = (P("vir", "occ"), P("occ", "vir"))
    return jax.shard_map(
        make_body(mesh.shape["occ"], mesh.shape["vir"]),
        mesh=mesh,
        in_specs=placed,
        out_specs=P("occ", "vir"),
        check_vma=False,
    )
```

```python
import jax
import jax.numpy as jnp
from jax import lax
from jax.sharding import PartitionSpec as P

HIGH = lax.Precision.HIGH


def _pairs(n, dest):
    return [(k, dest(k)) for k in range(n)]


def make_body(n_occ, n_vir):
    ny = n_vir // 4
    nx = n_occ // 2

    def y_shift(s):
        def dest(j):
            zl, y, c = j // (2 * ny), (j // 2) % ny, j % 2
            return zl * (2 * ny) + ((y + s) % ny) * 2 + c

        return _pairs(n_vir, dest)

    def x_shift(s):
        return _pairs(n_occ, lambda i: (i // nx) * nx + (i % nx + s) % nx)

    z_swap = _pairs(n_vir, lambda j: j ^ (2 * ny))
    core_swap = _pairs(n_vir, lambda j: j ^ 1)
    zhi_swap = _pairs(n_occ, lambda i: (i + nx) % n_occ)

    def matmul(a, b):
        return jnp.dot(a, b, preferred_element_type=jnp.float32, precision=HIGH)

    def body(amplitudes, integrals):
        rows, cd = amplitudes.shape
        me = lax.axis_index("vir")
        zl, y, c = me // (2 * ny), (me // 2) % ny, me % 2

        half = 0.5 * integrals
        res_own = matmul(amplitudes, half)
        own, res_own = lax.optimization_barrier((amplitudes, res_own))
        z1 = lax.ppermute(own, "vir", z_swap)
        ym1 = lax.ppermute(own, "vir", y_shift(1))
        yp1 = lax.ppermute(own, "vir", y_shift(-1))
        z2 = lax.ppermute(yp1, "vir", z_swap)
        yp2 = lax.ppermute(yp1, "vir", y_shift(-1))
        ym1z = lax.ppermute(z1, "vir", y_shift(1))
        z3 = lax.ppermute(yp2, "vir", z_swap)
        local = jnp.concatenate([own, z1, yp1, z2, yp2, z3, ym1, ym1z], axis=0)
        res_l = jnp.concatenate([res_own, matmul(local[rows:], half)], axis=0)
        local, res_l = lax.optimization_barrier((local, res_l))
        res_l = res_l.reshape(8, rows, -1)
        other = lax.ppermute(local, "vir", core_swap)
        res_o = matmul(other, half).reshape(8, rows, -1)

        def out_block(r):
            dy = (r % nx - y) % ny
            dz = (r // nx) ^ zl
            k = dy * 2 + dz
            lk = lax.dynamic_index_in_dim(res_l, k, 0, keepdims=False)
            ok = lax.dynamic_index_in_dim(res_o, k, 0, keepdims=False)
            first = jnp.where(c == 0, lk, ok)
            second = jnp.where(c == 0, ok, lk)
            return jnp.concatenate([first, second], axis=0)

        mo = lax.axis_index("occ")
        x, zh = mo % nx, mo // nx
        sa = out_block((x - 1) % nx)
        sb = out_block(nx + (x + 1) % nx)
        for s in range(1, nx):
            sa = lax.ppermute(sa, "occ", x_shift(1)) + out_block((x - s - 1) % nx)
            sb = lax.ppermute(sb, "occ", x_shift(-1)) + out_block(nx + (x + s + 1) % nx)
        keep = jnp.where(zh == 0, sa, sb)
        send = jnp.where(zh == 0, sb, sa)
        return keep + lax.ppermute(send, "occ", zhi_swap)

    return body


def solution(mesh):
    placed = (P("vir", "occ"), P("occ", "vir"))
    return jax.shard_map(
        make_body(mesh.shape["occ"], mesh.shape["vir"]),
        mesh=mesh,
        in_specs=placed,
        out_specs=P("occ", "vir"),
        check_vma=False,
    )
```

```python
import jax
import jax.numpy as jnp
from jax import lax
from jax.sharding import PartitionSpec as P

HIGH = lax.Precision.HIGH


def _pairs(n, dest):
    return [(k, dest(k)) for k in range(n)]


def make_body(n_occ, n_vir):
    ny = n_vir // 4
    nx = n_occ // 2

    def y_shift(s):
        def dest(j):
            zl, y, c = j // (2 * ny), (j // 2) % ny, j % 2
            return zl * (2 * ny) + ((y + s) % ny) * 2 + c

        return _pairs(n_vir, dest)

    def x_shift(s):
        return _pairs(n_occ, lambda i: (i // nx) * nx + (i % nx + s) % nx)

    z_swap = _pairs(n_vir, lambda j: j ^ (2 * ny))
    core_swap = _pairs(n_vir, lambda j: j ^ 1)
    zhi_swap = _pairs(n_occ, lambda i: (i + nx) % n_occ)

    def matmul(a, b):
        return jnp.dot(a, b, preferred_element_type=jnp.float32, precision=HIGH)

    def body(amplitudes, integrals):
        rows, cd = amplitudes.shape
        me = lax.axis_index("vir")
        zl, y, c = me // (2 * ny), (me // 2) % ny, me % 2

        half = 0.5 * integrals
        res_own = matmul(amplitudes, half)
        own, res_own = lax.optimization_barrier((amplitudes, res_own))
        z1 = lax.ppermute(own, "vir", z_swap)
        ym1 = lax.ppermute(own, "vir", y_shift(1))
        yp1 = lax.ppermute(own, "vir", y_shift(-1))
        z2 = lax.ppermute(yp1, "vir", z_swap)
        yp2 = lax.ppermute(yp1, "vir", y_shift(-1))
        ym1z = lax.ppermute(z1, "vir", y_shift(1))
        z3 = lax.ppermute(yp2, "vir", z_swap)
        local = jnp.concatenate([own, z1, yp1, z2, yp2, z3, ym1, ym1z], axis=0)
        res_l = jnp.concatenate([res_own, matmul(local[rows:], half)], axis=0)
        local, res_l = lax.optimization_barrier((local, res_l))
        res_l = res_l.reshape(8, rows, -1)
        other = lax.ppermute(local, "vir", core_swap)
        mo = lax.axis_index("occ")
        x, zh = mo % nx, mo // nx

        def ring(res):
            def half_block(r):
                k = ((r % nx - y) % ny) * 2 + ((r // nx) ^ zl)
                return lax.dynamic_index_in_dim(res, k, 0, keepdims=False)

            sa = half_block((x - 1) % nx)
            sb = half_block(nx + (x + 1) % nx)
            for s in range(1, nx):
                sa = lax.ppermute(sa, "occ", x_shift(1)) + half_block((x - s - 1) % nx)
                sb = lax.ppermute(sb, "occ", x_shift(-1)) + half_block(nx + (x + s + 1) % nx)
            keep = jnp.where(zh == 0, sa, sb)
            send = jnp.where(zh == 0, sb, sa)
            return keep + lax.ppermute(send, "occ", zhi_swap)

        sum_l = ring(res_l)
        res_o = matmul(other, half).reshape(8, rows, -1)
        sum_o = ring(res_o)
        first = jnp.where(c == 0, sum_l, sum_o)
        second = jnp.where(c == 0, sum_o, sum_l)
        return jnp.concatenate([first, second], axis=0)

    return body


def solution(mesh):
    placed = (P("vir", "occ"), P("occ", "vir"))
    return jax.shard_map(
        make_body(mesh.shape["occ"], mesh.shape["vir"]),
        mesh=mesh,
        in_specs=placed,
        out_specs=P("occ", "vir"),
        check_vma=False,
    )
```

```python
import jax
import jax.numpy as jnp
from jax import lax
from jax.sharding import PartitionSpec as P

HIGH = lax.Precision.HIGH


def _pairs(n, dest):
    return [(k, dest(k)) for k in range(n)]


def make_body(n_occ, n_vir):
    ny = n_vir // 4
    nx = n_occ // 2

    def y_shift(s):
        def dest(j):
            zl, y, c = j // (2 * ny), (j // 2) % ny, j % 2
            return zl * (2 * ny) + ((y + s) % ny) * 2 + c

        return _pairs(n_vir, dest)

    def x_shift(s):
        return _pairs(n_occ, lambda i: (i // nx) * nx + (i % nx + s) % nx)

    z_swap = _pairs(n_vir, lambda j: j ^ (2 * ny))
    core_swap = _pairs(n_vir, lambda j: j ^ 1)
    zhi_swap = _pairs(n_occ, lambda i: (i + nx) % n_occ)

    def matmul(a, b):
        return jnp.dot(a, b, preferred_element_type=jnp.float32, precision=HIGH)

    def body(amplitudes, integrals):
        rows, cd = amplitudes.shape
        me = lax.axis_index("vir")
        zl, y, c = me // (2 * ny), (me // 2) % ny, me % 2

        half = 0.5 * integrals
        own = amplitudes
        z1 = lax.ppermute(own, "vir", z_swap)
        ym1 = lax.ppermute(own, "vir", y_shift(1))
        yp1 = lax.ppermute(own, "vir", y_shift(-1))
        z2 = lax.ppermute(yp1, "vir", z_swap)
        yp2 = lax.ppermute(yp1, "vir", y_shift(-1))
        ym1z = lax.ppermute(z1, "vir", y_shift(1))
        z3 = lax.ppermute(yp2, "vir", z_swap)
        local = jnp.concatenate([own, z1, yp1, z2, yp2, z3, ym1, ym1z], axis=0)
        res_l = matmul(local, half)
        res_l = res_l.reshape(8, rows, -1)
        other = lax.ppermute(local, "vir", core_swap)
        mo = lax.axis_index("occ")
        x, zh = mo % nx, mo // nx

        def ring(res):
            def half_block(r):
                k = ((r % nx - y) % ny) * 2 + ((r // nx) ^ zl)
                return lax.dynamic_index_in_dim(res, k, 0, keepdims=False)

            sa = half_block((x - 1) % nx)
            sb = half_block(nx + (x + 1) % nx)
            for s in range(1, nx):
                sa = lax.ppermute(sa, "occ", x_shift(1)) + half_block((x - s - 1) % nx)
                sb = lax.ppermute(sb, "occ", x_shift(-1)) + half_block(nx + (x + s + 1) % nx)
            keep = jnp.where(zh == 0, sa, sb)
            send = jnp.where(zh == 0, sb, sa)
            return keep + lax.ppermute(send, "occ", zhi_swap)

        sum_l = ring(res_l)
        res_o = matmul(other, half).reshape(8, rows, -1)
        sum_o = ring(res_o)
        first = jnp.where(c == 0, sum_l, sum_o)
        second = jnp.where(c == 0, sum_o, sum_l)
        return jnp.concatenate([first, second], axis=0)

    return body


def solution(mesh):
    placed = (P("vir", "occ"), P("occ", "vir"))
    return jax.shard_map(
        make_body(mesh.shape["occ"], mesh.shape["vir"]),
        mesh=mesh,
        in_specs=placed,
        out_specs=P("occ", "vir"),
        check_vma=False,
    )
```

```python
import jax
import jax.numpy as jnp
from jax import lax
from jax.sharding import PartitionSpec as P

HIGH = lax.Precision.HIGH


def _pairs(n, dest):
    return [(k, dest(k)) for k in range(n)]


def make_body(n_occ, n_vir):
    ny = n_vir // 4
    nx = n_occ // 2

    def y_shift(s):
        def dest(j):
            zl, y, c = j // (2 * ny), (j // 2) % ny, j % 2
            return zl * (2 * ny) + ((y + s) % ny) * 2 + c

        return _pairs(n_vir, dest)

    def x_shift(s):
        return _pairs(n_occ, lambda i: (i // nx) * nx + (i % nx + s) % nx)

    z_swap = _pairs(n_vir, lambda j: j ^ (2 * ny))
    core_swap = _pairs(n_vir, lambda j: j ^ 1)
    zhi_swap = _pairs(n_occ, lambda i: (i + nx) % n_occ)

    def matmul(a, b):
        return jnp.dot(a, b, preferred_element_type=jnp.float32, precision=HIGH)

    def body(amplitudes, integrals):
        rows, cd = amplitudes.shape
        me = lax.axis_index("vir")
        zl, y, c = me // (2 * ny), (me // 2) % ny, me % 2

        half = 0.5 * integrals
        own = amplitudes
        z1 = lax.ppermute(own, "vir", z_swap)
        ym1 = lax.ppermute(own, "vir", y_shift(1))
        yp1 = lax.ppermute(own, "vir", y_shift(-1))
        z2 = lax.ppermute(yp1, "vir", z_swap)
        yp2 = lax.ppermute(yp1, "vir", y_shift(-1))
        ym1z = lax.ppermute(z1, "vir", y_shift(1))
        z3 = lax.ppermute(yp2, "vir", z_swap)
        local = jnp.concatenate([own, z1, yp1, z2, yp2, z3, ym1, ym1z], axis=0)
        res_l = matmul(local, half)
        res_l = res_l.reshape(8, rows, -1)
        other = lax.ppermute(local, "vir", core_swap)
        mo = lax.axis_index("occ")
        x, zh = mo % nx, mo // nx

        def ring(res):
            def half_block(r):
                k = ((r % nx - y) % ny) * 2 + ((r // nx) ^ zl)
                return lax.dynamic_index_in_dim(res, k, 0, keepdims=False)

            def a_blk(t):
                return half_block(t % nx)

            def b_blk(t):
                return half_block(nx + t % nx)

            p1 = lax.ppermute(a_blk(x + 2), "occ", x_shift(-1))
            q1 = lax.ppermute(b_blk(x + 2), "occ", x_shift(1))
            to_m = jnp.concatenate([a_blk(x + nx - 1) + p1, b_blk(x + nx - 1)], axis=0)
            to_p = jnp.concatenate([a_blk(x + 1), b_blk(x + 1) + q1], axis=0)
            total = (
                lax.ppermute(to_m, "occ", x_shift(-1))
                + lax.ppermute(to_p, "occ", x_shift(1))
                + jnp.concatenate([a_blk(x), b_blk(x)], axis=0)
            )
            keep = jnp.where(zh == 0, total[:rows], total[rows:])
            send = jnp.where(zh == 0, total[rows:], total[:rows])
            return keep + lax.ppermute(send, "occ", zhi_swap)

        sum_l = ring(res_l)
        res_o = matmul(other, half).reshape(8, rows, -1)
        sum_o = ring(res_o)
        first = jnp.where(c == 0, sum_l, sum_o)
        second = jnp.where(c == 0, sum_o, sum_l)
        return jnp.concatenate([first, second], axis=0)

    return body


def solution(mesh):
    placed = (P("vir", "occ"), P("occ", "vir"))
    return jax.shard_map(
        make_body(mesh.shape["occ"], mesh.shape["vir"]),
        mesh=mesh,
        in_specs=placed,
        out_specs=P("occ", "vir"),
        check_vma=False,
    )
```

```python
import jax
import jax.numpy as jnp
from jax import lax
from jax.sharding import PartitionSpec as P

HIGH = lax.Precision.HIGH


def _pairs(n, dest):
    return [(k, dest(k)) for k in range(n)]


def make_body(n_occ, n_vir):
    ny = n_vir // 4
    nx = n_occ // 2

    def y_shift(s):
        def dest(j):
            zl, y, c = j // (2 * ny), (j // 2) % ny, j % 2
            return zl * (2 * ny) + ((y + s) % ny) * 2 + c

        return _pairs(n_vir, dest)

    def x_shift(s):
        return _pairs(n_occ, lambda i: (i // nx) * nx + (i % nx + s) % nx)

    z_swap = _pairs(n_vir, lambda j: j ^ (2 * ny))
    core_swap = _pairs(n_vir, lambda j: j ^ 1)
    zhi_swap = _pairs(n_occ, lambda i: (i + nx) % n_occ)

    def matmul(a, b):
        return jnp.dot(a, b, preferred_element_type=jnp.float32, precision=HIGH)

    def body(amplitudes, integrals):
        rows, cd = amplitudes.shape
        me = lax.axis_index("vir")
        zl, y, c = me // (2 * ny), (me // 2) % ny, me % 2

        half = 0.5 * integrals
        own = amplitudes
        z1 = lax.ppermute(own, "vir", z_swap)
        ym1 = lax.ppermute(own, "vir", y_shift(1))
        yp1 = lax.ppermute(own, "vir", y_shift(-1))
        z2 = lax.ppermute(yp1, "vir", z_swap)
        yp2 = lax.ppermute(yp1, "vir", y_shift(-1))
        ym1z = lax.ppermute(z1, "vir", y_shift(1))
        z3 = lax.ppermute(yp2, "vir", z_swap)
        local = jnp.concatenate([own, z1, yp1, z2, yp2, z3, ym1, ym1z], axis=0)
        res_l = matmul(local, half)
        res_l = res_l.reshape(8, rows, -1)
        other = lax.ppermute(local, "vir", core_swap)
        mo = lax.axis_index("occ")
        x, zh = mo % nx, mo // nx

        def ring(res):
            def half_block(r):
                k = ((r % nx - y) % ny) * 2 + ((r // nx) ^ zl)
                return lax.dynamic_index_in_dim(res, k, 0, keepdims=False)

            def a_blk(t):
                return half_block(t % nx)

            def b_blk(t):
                return half_block(nx + t % nx)

            p1 = lax.ppermute(a_blk(x + 2), "occ", x_shift(-1))
            q1 = lax.ppermute(b_blk(x + 2), "occ", x_shift(1))
            to_m = jnp.concatenate([a_blk(x + nx - 1) + p1, b_blk(x + nx - 1)], axis=0)
            to_p = jnp.concatenate([a_blk(x + 1), b_blk(x + 1) + q1], axis=0)
            total = (
                lax.ppermute(to_m, "occ", x_shift(-1))
                + lax.ppermute(to_p, "occ", x_shift(1))
                + jnp.concatenate([a_blk(x), b_blk(x)], axis=0)
            )
            keep = jnp.where(zh == 0, total[:rows], total[rows:])
            send = jnp.where(zh == 0, total[rows:], total[:rows])
            return keep + lax.ppermute(send, "occ", zhi_swap)

        res_o = matmul(other, half).reshape(8, rows, -1)
        res_l, res_o = lax.optimization_barrier((res_l, res_o))
        sum_l = ring(res_l)
        sum_o = ring(res_o)
        first = jnp.where(c == 0, sum_l, sum_o)
        second = jnp.where(c == 0, sum_o, sum_l)
        return jnp.concatenate([first, second], axis=0)

    return body


def solution(mesh):
    placed = (P("vir", "occ"), P("occ", "vir"))
    return jax.shard_map(
        make_body(mesh.shape["occ"], mesh.shape["vir"]),
        mesh=mesh,
        in_specs=placed,
        out_specs=P("occ", "vir"),
        check_vma=False,
    )
```

```python
import jax
import jax.numpy as jnp
from jax import lax
from jax.sharding import PartitionSpec as P

HIGH = lax.Precision.HIGH


def _pairs(n, dest):
    return [(k, dest(k)) for k in range(n)]


def make_body(n_occ, n_vir):
    ny = n_vir // 4
    nx = n_occ // 2

    def y_shift(s):
        def dest(j):
            zl, y, c = j // (2 * ny), (j // 2) % ny, j % 2
            return zl * (2 * ny) + ((y + s) % ny) * 2 + c

        return _pairs(n_vir, dest)

    def x_shift(s):
        return _pairs(n_occ, lambda i: (i // nx) * nx + (i % nx + s) % nx)

    z_swap = _pairs(n_vir, lambda j: j ^ (2 * ny))
    core_swap = _pairs(n_vir, lambda j: j ^ 1)
    zhi_swap = _pairs(n_occ, lambda i: (i + nx) % n_occ)

    def matmul(a, b):
        return jnp.dot(a, b, preferred_element_type=jnp.float32, precision=HIGH)

    def body(amplitudes, integrals):
        rows, cd = amplitudes.shape
        me = lax.axis_index("vir")
        zl, y, c = me // (2 * ny), (me // 2) % ny, me % 2

        half = 0.5 * integrals
        own = amplitudes
        z1 = lax.ppermute(own, "vir", z_swap)
        ym1 = lax.ppermute(own, "vir", y_shift(1))
        yp1 = lax.ppermute(own, "vir", y_shift(-1))
        z2 = lax.ppermute(yp1, "vir", z_swap)
        yp2 = lax.ppermute(yp1, "vir", y_shift(-1))
        ym1z = lax.ppermute(z1, "vir", y_shift(1))
        z3 = lax.ppermute(yp2, "vir", z_swap)
        local = jnp.concatenate([own, z1, yp1, z2, yp2, z3, ym1, ym1z], axis=0)
        res_l = matmul(local, half)
        res_l = res_l.reshape(8, rows, -1)
        other = lax.ppermute(local, "vir", core_swap)
        mo = lax.axis_index("occ")
        x, zh = mo % nx, mo // nx

        def reduce_both(res_l, res_o):
            def half_block(r):
                k = ((r % nx - y) % ny) * 2 + ((r // nx) ^ zl)
                return jnp.stack(
                    [
                        lax.dynamic_index_in_dim(res_l, k, 0, keepdims=False),
                        lax.dynamic_index_in_dim(res_o, k, 0, keepdims=False),
                    ]
                )

            def a_blk(t):
                return half_block(t % nx)

            def b_blk(t):
                return half_block(nx + t % nx)

            p1 = lax.ppermute(a_blk(x + 2), "occ", x_shift(-1))
            q1 = lax.ppermute(b_blk(x + 2), "occ", x_shift(1))
            to_m = jnp.concatenate([a_blk(x + nx - 1) + p1, b_blk(x + nx - 1)], axis=1)
            to_p = jnp.concatenate([a_blk(x + 1), b_blk(x + 1) + q1], axis=1)
            total = (
                lax.ppermute(to_m, "occ", x_shift(-1))
                + lax.ppermute(to_p, "occ", x_shift(1))
                + jnp.concatenate([a_blk(x), b_blk(x)], axis=1)
            )
            keep = jnp.where(zh == 0, total[:, :rows], total[:, rows:])
            send = jnp.where(zh == 0, total[:, rows:], total[:, :rows])
            return keep + lax.ppermute(send, "occ", zhi_swap)

        res_o = matmul(other, half).reshape(8, rows, -1)
        res_l, res_o = lax.optimization_barrier((res_l, res_o))
        sums = reduce_both(res_l, res_o)
        first = jnp.where(c == 0, sums[0], sums[1])
        second = jnp.where(c == 0, sums[1], sums[0])
        return jnp.concatenate([first, second], axis=0)

    return body


def solution(mesh):
    placed = (P("vir", "occ"), P("occ", "vir"))
    return jax.shard_map(
        make_body(mesh.shape["occ"], mesh.shape["vir"]),
        mesh=mesh,
        in_specs=placed,
        out_specs=P("occ", "vir"),
        check_vma=False,
    )
```

```python
import jax
import jax.numpy as jnp
from jax import lax
from jax.sharding import PartitionSpec as P

HIGH = lax.Precision.HIGH


def _pairs(n, dest):
    return [(k, dest(k)) for k in range(n)]


def make_body(n_occ, n_vir):
    ny = n_vir // 4
    nx = n_occ // 2

    def y_shift(s):
        def dest(j):
            zl, y, c = j // (2 * ny), (j // 2) % ny, j % 2
            return zl * (2 * ny) + ((y + s) % ny) * 2 + c

        return _pairs(n_vir, dest)

    def x_shift(s):
        return _pairs(n_occ, lambda i: (i // nx) * nx + (i % nx + s) % nx)

    z_swap = _pairs(n_vir, lambda j: j ^ (2 * ny))
    core_swap = _pairs(n_vir, lambda j: j ^ 1)
    zhi_swap = _pairs(n_occ, lambda i: (i + nx) % n_occ)

    def matmul(a, b):
        return jnp.dot(a, b, preferred_element_type=jnp.float32, precision=HIGH)

    def body(amplitudes, integrals):
        rows, cd = amplitudes.shape
        me = lax.axis_index("vir")
        zl, y, c = me // (2 * ny), (me // 2) % ny, me % 2

        half = 0.5 * integrals
        own = amplitudes
        z1 = lax.ppermute(own, "vir", z_swap)
        ym1 = lax.ppermute(own, "vir", y_shift(1))
        yp1 = lax.ppermute(own, "vir", y_shift(-1))
        z2 = lax.ppermute(yp1, "vir", z_swap)
        yp2 = lax.ppermute(yp1, "vir", y_shift(-1))
        ym1z = lax.ppermute(z1, "vir", y_shift(1))
        z3 = lax.ppermute(yp2, "vir", z_swap)
        local = jnp.concatenate([own, z1, yp1, z2, yp2, z3, ym1, ym1z], axis=0)
        res_l = matmul(local, half)
        res_l = res_l.reshape(8, rows, -1)
        other = lax.ppermute(local, "vir", core_swap)
        mo = lax.axis_index("occ")
        x, zh = mo % nx, mo // nx

        def reduce_both(res_l, res_o):
            def half_block(r):
                k = ((r % nx - y) % ny) * 2 + ((r // nx) ^ zl)
                return jnp.stack(
                    [
                        lax.dynamic_index_in_dim(res_l, k, 0, keepdims=False),
                        lax.dynamic_index_in_dim(res_o, k, 0, keepdims=False),
                    ]
                )

            def a_blk(t):
                return half_block(t % nx)

            def b_blk(t):
                return half_block(nx + t % nx)

            p1 = lax.ppermute(a_blk(x + 2), "occ", x_shift(-1))
            q1 = lax.ppermute(b_blk(x + 2), "occ", x_shift(1))
            to_m_a, to_m_b = a_blk(x + nx - 1) + p1, b_blk(x + nx - 1)
            to_p_a, to_p_b = a_blk(x + 1), b_blk(x + 1) + q1
            low = zh == 0
            got_send = (
                lax.ppermute(jnp.where(low, to_m_b, to_m_a), "occ", x_shift(-1))
                + lax.ppermute(jnp.where(low, to_p_b, to_p_a), "occ", x_shift(1))
                + jnp.where(low, b_blk(x), a_blk(x))
            )
            from_zhi = lax.ppermute(got_send, "occ", zhi_swap)
            got_keep = (
                lax.ppermute(jnp.where(low, to_m_a, to_m_b), "occ", x_shift(-1))
                + lax.ppermute(jnp.where(low, to_p_a, to_p_b), "occ", x_shift(1))
                + jnp.where(low, a_blk(x), b_blk(x))
            )
            return got_keep + from_zhi

        res_o = matmul(other, half).reshape(8, rows, -1)
        res_l, res_o = lax.optimization_barrier((res_l, res_o))
        sums = reduce_both(res_l, res_o)
        first = jnp.where(c == 0, sums[0], sums[1])
        second = jnp.where(c == 0, sums[1], sums[0])
        return jnp.concatenate([first, second], axis=0)

    return body


def solution(mesh):
    placed = (P("vir", "occ"), P("occ", "vir"))
    return jax.shard_map(
        make_body(mesh.shape["occ"], mesh.shape["vir"]),
        mesh=mesh,
        in_specs=placed,
        out_specs=P("occ", "vir"),
        check_vma=False,
    )
```

```python
import jax
import jax.numpy as jnp
from jax import lax
from jax.sharding import PartitionSpec as P

HIGH = lax.Precision.HIGH


def _pairs(n, dest):
    return [(k, dest(k)) for k in range(n)]


def make_body(n_occ, n_vir):
    ny = n_vir // 4
    nx = n_occ // 2

    def y_shift(s):
        def dest(j):
            zl, y, c = j // (2 * ny), (j // 2) % ny, j % 2
            return zl * (2 * ny) + ((y + s) % ny) * 2 + c

        return _pairs(n_vir, dest)

    def x_shift(s):
        return _pairs(n_occ, lambda i: (i // nx) * nx + (i % nx + s) % nx)

    z_swap = _pairs(n_vir, lambda j: j ^ (2 * ny))
    core_swap = _pairs(n_vir, lambda j: j ^ 1)
    zhi_swap = _pairs(n_occ, lambda i: (i + nx) % n_occ)

    def matmul(a, b):
        return jnp.dot(a, b, preferred_element_type=jnp.float32, precision=HIGH)

    def body(amplitudes, integrals):
        rows, cd = amplitudes.shape
        me = lax.axis_index("vir")
        zl, y, c = me // (2 * ny), (me // 2) % ny, me % 2

        half = 0.5 * integrals
        own = amplitudes
        z1 = lax.ppermute(own, "vir", z_swap)
        ym1 = lax.ppermute(own, "vir", y_shift(1))
        yp1 = lax.ppermute(own, "vir", y_shift(-1))
        z2 = lax.ppermute(yp1, "vir", z_swap)
        yp2 = lax.ppermute(yp1, "vir", y_shift(-1))
        ym1z = lax.ppermute(z1, "vir", y_shift(1))
        z3 = lax.ppermute(yp2, "vir", z_swap)
        local = jnp.concatenate([own, z1, yp1, z2, yp2, z3, ym1, ym1z], axis=0)
        res_l = matmul(local, half)
        res_l = res_l.reshape(8, rows, -1)
        other = lax.ppermute(local, "vir", core_swap)
        mo = lax.axis_index("occ")
        x, zh = mo % nx, mo // nx

        def reduce_both(res_l, res_o, far_o):
            def half_block(r):
                k = ((r % nx - y) % ny) * 2 + ((r // nx) ^ zl)
                return jnp.stack(
                    [
                        lax.dynamic_index_in_dim(res_l, k, 0, keepdims=False),
                        lax.dynamic_index_in_dim(res_o, k, 0, keepdims=False),
                    ]
                )

            def a_blk(t):
                return half_block(t % nx)

            def b_blk(t):
                return half_block(nx + t % nx)

            far_l = lax.dynamic_index_in_dim(res_l, slot((x + 2) % nx), 0, keepdims=False)
            far_lb = lax.dynamic_index_in_dim(res_l, slot(nx + (x + 2) % nx), 0, keepdims=False)
            p1 = lax.ppermute(jnp.stack([far_l, far_o[:rows]]), "occ", x_shift(-1))
            q1 = lax.ppermute(jnp.stack([far_lb, far_o[rows:]]), "occ", x_shift(1))
            to_m_a, to_m_b = a_blk(x + nx - 1) + p1, b_blk(x + nx - 1)
            to_p_a, to_p_b = a_blk(x + 1), b_blk(x + 1) + q1
            low = zh == 0
            got_send = (
                lax.ppermute(jnp.where(low, to_m_b, to_m_a), "occ", x_shift(-1))
                + lax.ppermute(jnp.where(low, to_p_b, to_p_a), "occ", x_shift(1))
                + jnp.where(low, b_blk(x), a_blk(x))
            )
            from_zhi = lax.ppermute(got_send, "occ", zhi_swap)
            got_keep = (
                lax.ppermute(jnp.where(low, to_m_a, to_m_b), "occ", x_shift(-1))
                + lax.ppermute(jnp.where(low, to_p_a, to_p_b), "occ", x_shift(1))
                + jnp.where(low, a_blk(x), b_blk(x))
            )
            return got_keep + from_zhi

        def slot(r):
            return ((r % nx - y) % ny) * 2 + ((r // nx) ^ zl)

        blocks = other.reshape(8, rows, -1)
        far = jnp.concatenate(
            [
                lax.dynamic_index_in_dim(blocks, slot((x + 2) % nx), 0, keepdims=False),
                lax.dynamic_index_in_dim(blocks, slot(nx + (x + 2) % nx), 0, keepdims=False),
            ],
            axis=0,
        )
        far_o = matmul(far, half)
        res_l, far_o = lax.optimization_barrier((res_l, far_o))
        res_o = matmul(other, half).reshape(8, rows, -1)
        sums = reduce_both(res_l, res_o, far_o)
        first = jnp.where(c == 0, sums[0], sums[1])
        second = jnp.where(c == 0, sums[1], sums[0])
        return jnp.concatenate([first, second], axis=0)

    return body


def solution(mesh):
    placed = (P("vir", "occ"), P("occ", "vir"))
    return jax.shard_map(
        make_body(mesh.shape["occ"], mesh.shape["vir"]),
        mesh=mesh,
        in_specs=placed,
        out_specs=P("occ", "vir"),
        check_vma=False,
    )
```

```python
import jax
import jax.numpy as jnp
from jax import lax
from jax.sharding import PartitionSpec as P

HIGH = lax.Precision.HIGH


def _pairs(n, dest):
    return [(k, dest(k)) for k in range(n)]


def make_body(n_occ, n_vir):
    ny = n_vir // 4
    nx = n_occ // 2

    def y_shift(s):
        def dest(j):
            zl, y, c = j // (2 * ny), (j // 2) % ny, j % 2
            return zl * (2 * ny) + ((y + s) % ny) * 2 + c

        return _pairs(n_vir, dest)

    def x_shift(s):
        return _pairs(n_occ, lambda i: (i // nx) * nx + (i % nx + s) % nx)

    z_swap = _pairs(n_vir, lambda j: j ^ (2 * ny))
    core_swap = _pairs(n_vir, lambda j: j ^ 1)
    zhi_swap = _pairs(n_occ, lambda i: (i + nx) % n_occ)

    def matmul(a, b):
        return jnp.dot(a, b, preferred_element_type=jnp.float32, precision=HIGH)

    def body(amplitudes, integrals):
        rows, cd = amplitudes.shape
        me = lax.axis_index("vir")
        zl, y, c = me // (2 * ny), (me // 2) % ny, me % 2

        half = 0.5 * integrals
        own = amplitudes
        z1 = lax.ppermute(own, "vir", z_swap)
        ym1 = lax.ppermute(own, "vir", y_shift(1))
        yp1 = lax.ppermute(own, "vir", y_shift(-1))
        z2 = lax.ppermute(yp1, "vir", z_swap)
        yp2 = lax.ppermute(yp1, "vir", y_shift(-1))
        ym1z = lax.ppermute(z1, "vir", y_shift(1))
        z3 = lax.ppermute(yp2, "vir", z_swap)
        local = jnp.concatenate([own, z1, yp1, z2, yp2, z3, ym1, ym1z], axis=0)
        res_l = matmul(local, half)
        res_l = res_l.reshape(8, rows, -1)
        other = lax.ppermute(local, "vir", core_swap)
        mo = lax.axis_index("occ")
        x, zh = mo % nx, mo // nx

        def reduce_both(res_l, res_o, far_o):
            def half_block(r):
                k = ((r % nx - y) % ny) * 2 + ((r // nx) ^ zl)
                return jnp.stack(
                    [
                        lax.dynamic_index_in_dim(res_l, k, 0, keepdims=False),
                        lax.dynamic_index_in_dim(res_o, k, 0, keepdims=False),
                    ]
                )

            def a_blk(t):
                return half_block(t % nx)

            def b_blk(t):
                return half_block(nx + t % nx)

            far_l = lax.dynamic_index_in_dim(res_l, slot((x + 2) % nx), 0, keepdims=False)
            far_lb = lax.dynamic_index_in_dim(res_l, slot(nx + (x + 2) % nx), 0, keepdims=False)
            p1 = lax.ppermute(jnp.stack([far_l, far_o[:rows]]), "occ", x_shift(-1))
            q1 = lax.ppermute(jnp.stack([far_lb, far_o[rows:]]), "occ", x_shift(1))
            to_m_a, to_m_b = a_blk(x + nx - 1) + p1, b_blk(x + nx - 1)
            to_p_a, to_p_b = a_blk(x + 1), b_blk(x + 1) + q1
            low = zh == 0
            got_send = (
                lax.ppermute(jnp.where(low, to_m_b, to_m_a), "occ", x_shift(-1))
                + lax.ppermute(jnp.where(low, to_p_b, to_p_a), "occ", x_shift(1))
                + jnp.where(low, b_blk(x), a_blk(x))
            )
            from_zhi = lax.ppermute(got_send, "occ", zhi_swap)
            got_keep = (
                lax.ppermute(jnp.where(low, to_m_a, to_m_b), "occ", x_shift(-1))
                + lax.ppermute(jnp.where(low, to_p_a, to_p_b), "occ", x_shift(1))
                + jnp.where(low, a_blk(x), b_blk(x))
            )
            return got_keep + from_zhi

        def slot(r):
            return ((r % nx - y) % ny) * 2 + ((r // nx) ^ zl)

        blocks = local.reshape(8, rows, -1)
        far = jnp.concatenate(
            [
                lax.dynamic_index_in_dim(blocks, slot((x + 2) % nx), 0, keepdims=False),
                lax.dynamic_index_in_dim(blocks, slot(nx + (x + 2) % nx), 0, keepdims=False),
            ],
            axis=0,
        )
        far_o = matmul(lax.ppermute(far, "vir", core_swap), half)
        res_l, far_o = lax.optimization_barrier((res_l, far_o))
        res_o = matmul(other, half).reshape(8, rows, -1)
        sums = reduce_both(res_l, res_o, far_o)
        first = jnp.where(c == 0, sums[0], sums[1])
        second = jnp.where(c == 0, sums[1], sums[0])
        return jnp.concatenate([first, second], axis=0)

    return body


def solution(mesh):
    placed = (P("vir", "occ"), P("occ", "vir"))
    return jax.shard_map(
        make_body(mesh.shape["occ"], mesh.shape["vir"]),
        mesh=mesh,
        in_specs=placed,
        out_specs=P("occ", "vir"),
        check_vma=False,
    )
```

```python
import jax
import jax.numpy as jnp
from jax import lax
from jax.sharding import PartitionSpec as P

HIGH = lax.Precision.HIGH


def _pairs(n, dest):
    return [(k, dest(k)) for k in range(n)]


def make_body(n_occ, n_vir):
    ny = n_vir // 4
    nx = n_occ // 2

    def y_shift(s):
        def dest(j):
            zl, y, c = j // (2 * ny), (j // 2) % ny, j % 2
            return zl * (2 * ny) + ((y + s) % ny) * 2 + c

        return _pairs(n_vir, dest)

    def x_shift(s):
        return _pairs(n_occ, lambda i: (i // nx) * nx + (i % nx + s) % nx)

    z_swap = _pairs(n_vir, lambda j: j ^ (2 * ny))
    core_swap = _pairs(n_vir, lambda j: j ^ 1)
    zhi_swap = _pairs(n_occ, lambda i: (i + nx) % n_occ)

    def matmul(a, b):
        return jnp.dot(a, b, preferred_element_type=jnp.float32, precision=HIGH)

    def body(amplitudes, integrals):
        rows, cd = amplitudes.shape
        me = lax.axis_index("vir")
        zl, y, c = me // (2 * ny), (me // 2) % ny, me % 2

        half = 0.5 * integrals
        own = amplitudes
        z1 = lax.ppermute(own, "vir", z_swap)
        ym1 = lax.ppermute(own, "vir", y_shift(1))
        yp1 = lax.ppermute(own, "vir", y_shift(-1))
        z2 = lax.ppermute(yp1, "vir", z_swap)
        yp2 = lax.ppermute(yp1, "vir", y_shift(-1))
        ym1z = lax.ppermute(z1, "vir", y_shift(1))
        z3 = lax.ppermute(yp2, "vir", z_swap)
        local = jnp.concatenate([own, z1, yp1, z2, yp2, z3, ym1, ym1z], axis=0)
        res_l = matmul(local, half)
        res_l = res_l.reshape(8, rows, -1)
        other = lax.ppermute(local, "vir", core_swap)
        mo = lax.axis_index("occ")
        x, zh = mo % nx, mo // nx

        def reduce_both(res_l, res_o, far_l, far_o):
            def half_block(r):
                k = ((r % nx - y) % ny) * 2 + ((r // nx) ^ zl)
                return jnp.stack(
                    [
                        lax.dynamic_index_in_dim(res_l, k, 0, keepdims=False),
                        lax.dynamic_index_in_dim(res_o, k, 0, keepdims=False),
                    ]
                )

            def a_blk(t):
                return half_block(t % nx)

            def b_blk(t):
                return half_block(nx + t % nx)

            p1 = lax.ppermute(jnp.stack([far_l[:rows], far_o[:rows]]), "occ", x_shift(-1))
            q1 = lax.ppermute(jnp.stack([far_l[rows:], far_o[rows:]]), "occ", x_shift(1))
            to_m_a, to_m_b = a_blk(x + nx - 1) + p1, b_blk(x + nx - 1)
            to_p_a, to_p_b = a_blk(x + 1), b_blk(x + 1) + q1
            low = zh == 0
            got_send = (
                lax.ppermute(jnp.where(low, to_m_b, to_m_a), "occ", x_shift(-1))
                + lax.ppermute(jnp.where(low, to_p_b, to_p_a), "occ", x_shift(1))
                + jnp.where(low, b_blk(x), a_blk(x))
            )
            from_zhi = lax.ppermute(got_send, "occ", zhi_swap)
            got_keep = (
                lax.ppermute(jnp.where(low, to_m_a, to_m_b), "occ", x_shift(-1))
                + lax.ppermute(jnp.where(low, to_p_a, to_p_b), "occ", x_shift(1))
                + jnp.where(low, a_blk(x), b_blk(x))
            )
            return got_keep + from_zhi

        def slot(r):
            return ((r % nx - y) % ny) * 2 + ((r // nx) ^ zl)

        blocks = local.reshape(8, rows, -1)
        far = jnp.concatenate(
            [
                lax.dynamic_index_in_dim(blocks, slot((x + 2) % nx), 0, keepdims=False),
                lax.dynamic_index_in_dim(blocks, slot(nx + (x + 2) % nx), 0, keepdims=False),
            ],
            axis=0,
        )
        far_o = matmul(lax.ppermute(far, "vir", core_swap), half)
        far_l = matmul(far, half)
        far_l, far_o = lax.optimization_barrier((far_l, far_o))
        res_o = matmul(other, half).reshape(8, rows, -1)
        sums = reduce_both(res_l, res_o, far_l, far_o)
        first = jnp.where(c == 0, sums[0], sums[1])
        second = jnp.where(c == 0, sums[1], sums[0])
        return jnp.concatenate([first, second], axis=0)

    return body


def solution(mesh):
    placed = (P("vir", "occ"), P("occ", "vir"))
    return jax.shard_map(
        make_body(mesh.shape["occ"], mesh.shape["vir"]),
        mesh=mesh,
        in_specs=placed,
        out_specs=P("occ", "vir"),
        check_vma=False,
    )
```
